256 devices in a mesh: dp: 16 (over x_hi, y, core), ctx: 16 (over x_lo, z).
Axes of the slice: x: 4 (x_hi: 2, x_lo: 2; x = x_hi * 2 + x_lo), y: 4, z: 8, core: 2. Of those that a mesh axis runs over, the one named last changes fastest.
Arguments:
- queries: bfloat16 [262144, 8, 128], P(('dp', 'ctx')), parts along dimension 0, may hold values from -6 to 6
- keys: bfloat16 [262144, 128], P(('dp', 'ctx')), parts along dimension 0, may hold values from -6 to 6
- values: bfloat16 [262144, 128], P(('dp', 'ctx')), parts along dimension 0, may hold values from -6 to 6
- output: bfloat16 [262144, 8, 128], P(('dp', 'ctx')), parts along dimension 0, may hold values from -6 to 6
- d_output: bfloat16 [262144, 8, 128], P(('dp', 'ctx')), parts along dimension 0, may hold values from -6 to 6
- block_lists: int32 [1024, 3], P('dp'), parts along dimension 0, may hold values from -1 to 63, as said below
Outputs:
- d_queries: bfloat16 [262144, 8, 128], P(('dp', 'ctx')), parts along dimension 0
- d_keys: bfloat16 [262144, 128], P(('dp', 'ctx')), parts along dimension 0
- d_values: bfloat16 [262144, 128], P(('dp', 'ctx')), parts along dimension 0
The draws below stay inside these ranges and needn't reach their ends.
There are 16 independent parts, one for each index of `dp`. The reference program is written for one: setup_inputs(seed, part) draws one part's arguments, and reference() takes and returns one part's arrays. A program takes and returns all parts, laid end to end along the dimension named above; each array names one. Nothing has to cross between parts.
Inputs may be any that keep to these rules, and one draw needn't show every extreme that they name: `block_lists`: row b: entry 0 is b itself; the other 2 entries are distinct blocks below b, or -1 where fewer than 2 blocks lie below b.
All inputs are finite; a program needn't handle non-finite values.
Results may differ from the reference program's by a relative error of at most 0.005.
Values may be sent and summed in bfloat16 or wider, within the bound.
No kernel may reach another device: no remote copies, remote signals or barrier semaphores. Data moves between devices by JAX's collectives and lax.ppermute only.
A program may use at most 192 MiB of HBM per device.

```python
import jax
import jax.numpy as jnp
from jax import lax

HQ = 8
HD = 128
BLK = 256
TOPK = 3
TOKENS = 16384


def draw_queries(key, part):
    drawn = jnp.clip(jax.random.normal(jax.random.fold_in(key, 3), (TOKENS, HQ, HD), jnp.float32), -6.0, 6.0)
    return drawn.astype(jnp.bfloat16)


def draw_keys(key, part):
    drawn = jnp.clip(jax.random.normal(jax.random.fold_in(key, 4), (TOKENS, HD), jnp.float32), -6.0, 6.0)
    return drawn.astype(jnp.bfloat16)


def draw_block_lists(key, part):
    nblocks = TOKENS // BLK
    jitter_draw = jax.random.randint(jax.random.fold_in(key, 21), (nblocks, nblocks), 0, 64)
    favour = jax.random.randint(jax.random.fold_in(key, 22), (nblocks,), 0, 4)
    column = jnp.arange(nblocks, dtype=jnp.int32)
    ranking = ((jitter_draw + 64 * favour[None, :]) * nblocks + column[None, :]).astype(jnp.int32)
    earlier = column[None, :] < column[:, None]
    ranking = jnp.where(earlier, ranking, -1)
    top_values, top_index = lax.top_k(ranking, TOPK - 1)
    chosen = jnp.where(top_values >= 0, top_index, -1)
    return jnp.concatenate([column[:, None], chosen], axis=1).astype(jnp.int32)


def shard_levels(stream_key, extent, shards, least, top_value):
    def one(axis_at, blocks):
        steps = jax.random.uniform(jax.random.fold_in(jax.random.fold_in(stream_key, 6), axis_at), (blocks,), jnp.float32, least / len(shards), top_value / len(shards))
        return jnp.repeat(jnp.exp(steps), extent[axis_at] // blocks).reshape((-1,) + (1,) * (len(extent) - axis_at - 1))

    level = one(*shards[0])
    for cut in shards[1:]:
        level = level * one(*cut)
    return level


def centred(own_key, dims, scale, reach, cuts=(), kind=jnp.bfloat16):
    entries = jax.random.normal(own_key, dims, jnp.float32) * scale
    if len(cuts) > 0:
        entries = shard_levels(own_key, dims, cuts, -0.22, 0.18) * entries
    return jnp.clip(entries, min=-reach, max=reach).astype(kind)


def setup_inputs(seed: int = 0, part: int = 0) -> dict:
    key_list = jax.random.split(jax.random.key(seed), 7)
    part_splits = jax.random.split(jax.random.fold_in(key_list[6], part), 7)
    queries = draw_queries(jax.random.fold_in(jax.random.fold_in(key_list[6], part), 71), part)
    keys = draw_keys(jax.random.fold_in(jax.random.fold_in(key_list[6], part), 71), part)
    values = centred(part_splits[2], (TOKENS, HD), 1.0, 6.0, ((0, 16),))
    output = centred(part_splits[3], (TOKENS, HQ, HD), 1.0, 6.0, ((0, 16),))
    d_output = centred(part_splits[4], (TOKENS, HQ, HD), 1.0, 6.0, ((0, 16),))
    block_lists = draw_block_lists(jax.random.fold_in(jax.random.fold_in(key_list[6], part), 71), part)
    return {"queries": queries, "keys": keys, "values": values, "output": output, "d_output": d_output, "block_lists": block_lists}


def reference(queries, keys, values, output, d_output, block_lists):
    nblocks = TOKENS // BLK
    scaling = HD ** -0.5
    query_f = queries.astype(jnp.float32).reshape(nblocks, BLK, HQ, HD)
    output_f = output.astype(jnp.float32).reshape(nblocks, BLK, HQ, HD)
    grad_f = d_output.astype(jnp.float32).reshape(nblocks, BLK, HQ, HD)
    key_f = keys.astype(jnp.float32)
    value_f = values.astype(jnp.float32)

    def one_block(carried, inputs):
        key_grad, value_grad = carried
        block_index, chosen, q_block, o_block, g_block = inputs
        starts = (jnp.maximum(chosen, 0) * BLK).astype(jnp.int32)
        key_sel = jnp.stack([lax.dynamic_slice_in_dim(key_f, starts[slot_index], BLK, 0) for slot_index in range(TOPK)])
        value_sel = jnp.stack([lax.dynamic_slice_in_dim(value_f, starts[slot_index], BLK, 0) for slot_index in range(TOPK)])
        raw = jnp.einsum("qhd,tkd->hqtk", q_block, key_sel) * scaling
        key_pos = starts[:, None] + jnp.arange(BLK, dtype=jnp.int32)[None, :]
        query_pos = (block_index * BLK + jnp.arange(BLK, dtype=jnp.int32)).astype(jnp.int32)
        allowed = (chosen >= 0)[None, :, None] & (key_pos[None, :, :] <= query_pos[:, None, None])
        scores = jnp.where(allowed[None], raw, -jnp.inf)
        top = jnp.max(scores, axis=(2, 3), keepdims=True)
        exps = jnp.exp(scores - top)
        prob = exps / jnp.sum(exps, axis=(2, 3), keepdims=True)
        prob_rounded = lax.optimization_barrier(prob.astype(jnp.bfloat16)).astype(jnp.float32)
        d_prob = jnp.einsum("qhd,tkd->hqtk", g_block, value_sel)
        delta = jnp.transpose(jnp.sum(g_block * o_block, axis=2))[:, :, None, None]
        d_scores = lax.optimization_barrier((prob * (d_prob - delta)).astype(jnp.bfloat16)).astype(jnp.float32)
        d_query = (jnp.einsum("hqtk,tkd->qhd", d_scores, key_sel) * scaling).astype(jnp.bfloat16)
        key_parts = jnp.einsum("hqtk,qhd->tkd", d_scores, q_block) * scaling
        value_parts = jnp.einsum("hqtk,qhd->tkd", prob_rounded, g_block)
        for slot_index in range(TOPK):
            begin = starts[slot_index]
            key_grad = lax.dynamic_update_slice_in_dim(key_grad, lax.dynamic_slice_in_dim(key_grad, begin, BLK, 0) + key_parts[slot_index], begin, 0)
            value_grad = lax.dynamic_update_slice_in_dim(value_grad, lax.dynamic_slice_in_dim(value_grad, begin, BLK, 0) + value_parts[slot_index], begin, 0)
        return (key_grad, value_grad), d_query

    zeros_grad = jnp.zeros((TOKENS, HD), jnp.float32)
    indices = jnp.arange(nblocks, dtype=jnp.int32)
    (key_grad, value_grad), d_query = lax.scan(one_block, (zeros_grad, zeros_grad), (indices, block_lists, query_f, output_f, grad_f))
    return d_query.reshape(TOKENS, HQ, HD), key_grad.astype(jnp.bfloat16), value_grad.astype(jnp.bfloat16)
```

```python
import jax
import jax.numpy as jnp
from jax import lax
from jax.sharding import PartitionSpec as P

BLK = 256
TOPK = 3


def shards(queries, keys, values, output, d_output, block_lists):
    shard_rows, heads, head_dim = queries.shape
    local_count = shard_rows // BLK
    my_index = lax.axis_index("ctx")
    scaling = head_dim ** (-0.5)
    total_blocks = block_lists.shape[0]

    paired = jnp.concatenate([keys, values], axis=1)
    everything = lax.all_gather(paired, "ctx", axis=0, tiled=True)
    all_blocks = everything.reshape(total_blocks, BLK, 2 * head_dim)

    global_blocks = my_index * local_count + jnp.arange(local_count, dtype=jnp.int32)
    chosen = block_lists[global_blocks]
    safe = jnp.maximum(chosen, 0)

    own = paired.reshape(local_count, 1, BLK, 2 * head_dim)
    far = all_blocks[safe[:, 1:]]
    kv_sel = jnp.concatenate([own, far], axis=1)
    key_sel = kv_sel[..., :head_dim]
    value_sel = kv_sel[..., head_dim:]

    q_b = queries.reshape(local_count, BLK, heads, head_dim)
    o_b = output.reshape(local_count, BLK, heads, head_dim)
    g_b = d_output.reshape(local_count, BLK, heads, head_dim)

    raw = jnp.einsum("bqhd,btkd->bhqtk", q_b, key_sel, preferred_element_type=jnp.float32) * scaling
    query_pos = global_blocks[:, None] * BLK + jnp.arange(BLK, dtype=jnp.int32)[None, :]
    key_pos = safe[:, :, None] * BLK + jnp.arange(BLK, dtype=jnp.int32)[None, None, :]
    allowed = (chosen >= 0)[:, None, :, None] & (key_pos[:, None, :, :] <= query_pos[:, :, None, None])
    scores = jnp.where(allowed[:, None], raw, -jnp.inf)
    top = jnp.max(scores, axis=(3, 4), keepdims=True)
    exps = jnp.exp(scores - top)
    prob = exps / jnp.sum(exps, axis=(3, 4), keepdims=True)

    d_prob = jnp.einsum("bqhd,btkd->bhqtk", g_b, value_sel, preferred_element_type=jnp.float32)
    delta = jnp.sum(g_b.astype(jnp.float32) * o_b.astype(jnp.float32), axis=3)
    delta = jnp.transpose(delta, (0, 2, 1))[:, :, :, None, None]
    d_scores = (prob * (d_prob - delta)).astype(jnp.bfloat16)
    prob_rounded = prob.astype(jnp.bfloat16)

    key_part = jnp.einsum("bhqtk,bqhd->btkd", d_scores, q_b, preferred_element_type=jnp.float32) * scaling
    value_part = jnp.einsum("bhqtk,bqhd->btkd", prob_rounded, g_b, preferred_element_type=jnp.float32)
    parts = jnp.concatenate([key_part, value_part], axis=3).reshape(local_count * TOPK, BLK, 2 * head_dim)
    grad_terms = jnp.zeros((total_blocks, BLK, 2 * head_dim), jnp.float32).at[safe.reshape(-1)].add(parts)
    grad_terms = grad_terms.reshape(total_blocks * BLK, 2 * head_dim)
    mine = lax.psum_scatter(grad_terms, "ctx", scatter_dimension=0, tiled=True)

    d_queries = jnp.einsum("bhqtk,btkd->bqhd", d_scores, key_sel, preferred_element_type=jnp.float32) * scaling
    d_queries = d_queries.astype(jnp.bfloat16).reshape(shard_rows, heads, head_dim)
    return (
        d_queries,
        mine[:, :head_dim].astype(jnp.bfloat16),
        mine[:, head_dim:].astype(jnp.bfloat16),
    )


def solution(mesh):
    return jax.shard_map(
        shards,
        mesh=mesh,
        in_specs=(
            P(("dp", "ctx"), None, None),
            P(("dp", "ctx"), None),
            P(("dp", "ctx"), None),
            P(("dp", "ctx"), None, None),
            P(("dp", "ctx"), None, None),
            P("dp", None),
        ),
        out_specs=(P(("dp", "ctx"), None, None), P(("dp", "ctx"), None), P(("dp", "ctx"), None)),
        check_vma=False,
    )
```

```python
import jax
import jax.numpy as jnp
from jax import lax
from jax.sharding import PartitionSpec as P

BLK = 256
TOPK = 3


def shards(queries, keys, values, output, d_output, block_lists):
    shard_rows, heads, head_dim = queries.shape
    local_count = shard_rows // BLK
    my_index = lax.axis_index("ctx")
    scaling = head_dim ** (-0.5)
    total_blocks = block_lists.shape[0]

    all_keys = lax.all_gather(keys, "ctx", axis=0, tiled=True).reshape(total_blocks, BLK, head_dim)
    all_values = lax.all_gather(values, "ctx", axis=0, tiled=True).reshape(total_blocks, BLK, head_dim)

    global_blocks = my_index * local_count + jnp.arange(local_count, dtype=jnp.int32)
    chosen = block_lists[global_blocks]
    safe = jnp.maximum(chosen, 0)

    key_sel = jnp.concatenate(
        [keys.reshape(local_count, 1, BLK, head_dim), all_keys[safe[:, 1:]]], axis=1
    )
    value_sel = jnp.concatenate(
        [values.reshape(local_count, 1, BLK, head_dim), all_values[safe[:, 1:]]], axis=1
    )

    q_b = queries.reshape(local_count, BLK, heads, head_dim)
    o_b = output.reshape(local_count, BLK, heads, head_dim)
    g_b = d_output.reshape(local_count, BLK, heads, head_dim)

    raw = jnp.einsum("bqhd,btkd->bhqtk", q_b, key_sel, preferred_element_type=jnp.float32) * scaling
    query_pos = global_blocks[:, None] * BLK + jnp.arange(BLK, dtype=jnp.int32)[None, :]
    key_pos = safe[:, :, None] * BLK + jnp.arange(BLK, dtype=jnp.int32)[None, None, :]
    allowed = (chosen >= 0)[:, None, :, None] & (key_pos[:, None, :, :] <= query_pos[:, :, None, None])
    scores = jnp.where(allowed[:, None], raw, -jnp.inf)
    top = jnp.max(scores, axis=(3, 4), keepdims=True)
    exps = jnp.exp(scores - top)
    prob = exps / jnp.sum(exps, axis=(3, 4), keepdims=True)

    d_prob = jnp.einsum("bqhd,btkd->bhqtk", g_b, value_sel, preferred_element_type=jnp.float32)
    delta = jnp.sum(g_b.astype(jnp.float32) * o_b.astype(jnp.float32), axis=3)
    delta = jnp.transpose(delta, (0, 2, 1))[:, :, :, None, None]
    d_scores = (prob * (d_prob - delta)).astype(jnp.bfloat16)
    prob_rounded = prob.astype(jnp.bfloat16)

    targets = safe.reshape(-1)

    def reduce_parts(part):
        part = part.reshape(local_count * TOPK, BLK, head_dim)
        terms = jnp.zeros((total_blocks, BLK, head_dim), jnp.float32).at[targets].add(part)
        terms = terms.reshape(total_blocks * BLK, head_dim)
        return lax.psum_scatter(terms, "ctx", scatter_dimension=0, tiled=True)

    value_part = jnp.einsum("bhqtk,bqhd->btkd", prob_rounded, g_b, preferred_element_type=jnp.float32)
    value_mine = reduce_parts(value_part)
    key_part = jnp.einsum("bhqtk,bqhd->btkd", d_scores, q_b, preferred_element_type=jnp.float32) * scaling
    key_mine = reduce_parts(key_part)

    d_queries = jnp.einsum("bhqtk,btkd->bqhd", d_scores, key_sel, preferred_element_type=jnp.float32) * scaling
    d_queries = d_queries.astype(jnp.bfloat16).reshape(shard_rows, heads, head_dim)
    return (
        d_queries,
        key_mine.astype(jnp.bfloat16),
        value_mine.astype(jnp.bfloat16),
    )


def solution(mesh):
    return jax.shard_map(
        shards,
        mesh=mesh,
        in_specs=(
            P(("dp", "ctx"), None, None),
            P(("dp", "ctx"), None),
            P(("dp", "ctx"), None),
            P(("dp", "ctx"), None, None),
            P(("dp", "ctx"), None, None),
            P("dp", None),
        ),
        out_specs=(P(("dp", "ctx"), None, None), P(("dp", "ctx"), None), P(("dp", "ctx"), None)),
        check_vma=False,
    )
```

```python
import jax
import jax.numpy as jnp
from jax import lax
from jax.sharding import PartitionSpec as P

BLK = 256
TOPK = 3


def shards(queries, keys, values, output, d_output, block_lists):
    shard_rows, heads, head_dim = queries.shape
    local_count = shard_rows // BLK
    my_index = lax.axis_index("ctx")
    scaling = head_dim ** (-0.5)
    total_blocks = block_lists.shape[0]

    paired = jnp.concatenate([keys, values], axis=1)
    everything = lax.all_gather(paired, "ctx", axis=0, tiled=True).reshape(total_blocks, BLK, 2 * head_dim)

    global_blocks = my_index * local_count + jnp.arange(local_count, dtype=jnp.int32)
    chosen = block_lists[global_blocks]
    safe = jnp.maximum(chosen, 0)

    far = everything[safe[:, 1:]]
    own_keys = keys.reshape(local_count, BLK, head_dim)
    own_values = values.reshape(local_count, BLK, head_dim)
    key_sel = jnp.concatenate([own_keys[:, None], far[..., :head_dim]], axis=1)

    q_b = queries.reshape(local_count, BLK, heads, head_dim)
    o_b = output.reshape(local_count, BLK, heads, head_dim)
    g_b = d_output.reshape(local_count, BLK, heads, head_dim)

    raw_own = jnp.einsum("bqhd,bkd->bhqk", q_b, own_keys, preferred_element_type=jnp.float32)
    raw_far = jnp.einsum("bqhd,btkd->bhqtk", q_b, far[..., :head_dim], preferred_element_type=jnp.float32)
    raw = jnp.concatenate([raw_own[:, :, :, None], raw_far], axis=3) * scaling
    query_pos = global_blocks[:, None] * BLK + jnp.arange(BLK, dtype=jnp.int32)[None, :]
    key_pos = safe[:, :, None] * BLK + jnp.arange(BLK, dtype=jnp.int32)[None, None, :]
    allowed = (chosen >= 0)[:, None, :, None] & (key_pos[:, None, :, :] <= query_pos[:, :, None, None])
    scores = jnp.where(allowed[:, None], raw, -jnp.inf)
    top = jnp.max(scores, axis=(3, 4), keepdims=True)
    exps = jnp.exp(scores - top)
    prob = exps / jnp.sum(exps, axis=(3, 4), keepdims=True)

    d_prob_own = jnp.einsum("bqhd,bkd->bhqk", g_b, own_values, preferred_element_type=jnp.float32)
    d_prob_far = jnp.einsum("bqhd,btkd->bhqtk", g_b, far[..., head_dim:], preferred_element_type=jnp.float32)
    d_prob = jnp.concatenate([d_prob_own[:, :, :, None], d_prob_far], axis=3)
    delta = jnp.sum(g_b.astype(jnp.float32) * o_b.astype(jnp.float32), axis=3)
    delta = jnp.transpose(delta, (0, 2, 1))[:, :, :, None, None]
    d_scores = (prob * (d_prob - delta)).astype(jnp.bfloat16)
    prob_rounded = prob.astype(jnp.bfloat16)

    targets = safe.reshape(-1)

    def reduce_parts(part):
        part = part.reshape(local_count * TOPK, BLK, head_dim)
        terms = jnp.zeros((total_blocks, BLK, head_dim), jnp.float32).at[targets].add(part)
        terms = terms.reshape(total_blocks * BLK, head_dim)
        return lax.psum_scatter(terms, "ctx", scatter_dimension=0, tiled=True)

    value_part = jnp.einsum("bhqtk,bqhd->btkd", prob_rounded, g_b, preferred_element_type=jnp.float32)
    value_mine = reduce_parts(value_part)
    key_part = jnp.einsum("bhqtk,bqhd->btkd", d_scores, q_b, preferred_element_type=jnp.float32) * scaling
    key_mine = reduce_parts(key_part)

    d_queries = jnp.einsum("bhqtk,btkd->bqhd", d_scores, key_sel, preferred_element_type=jnp.float32) * scaling
    d_queries = d_queries.astype(jnp.bfloat16).reshape(shard_rows, heads, head_dim)
    return (
        d_queries,
        key_mine.astype(jnp.bfloat16),
        value_mine.astype(jnp.bfloat16),
    )


def solution(mesh):
    return jax.shard_map(
        shards,
        mesh=mesh,
        in_specs=(
            P(("dp", "ctx"), None, None),
            P(("dp", "ctx"), None),
            P(("dp", "ctx"), None),
            P(("dp", "ctx"), None, None),
            P(("dp", "ctx"), None, None),
            P("dp", None),
        ),
        out_specs=(P(("dp", "ctx"), None, None), P(("dp", "ctx"), None), P(("dp", "ctx"), None)),
        check_vma=False,
    )
```

```python
import jax
import jax.numpy as jnp
from jax import lax
from jax.sharding import PartitionSpec as P

BLK = 256
TOPK = 3


def shards(queries, keys, values, output, d_output, block_lists):
    shard_rows, heads, head_dim = queries.shape
    local_count = shard_rows // BLK
    my_index = lax.axis_index("ctx")
    scaling = head_dim ** (-0.5)
    total_blocks = block_lists.shape[0]

    paired = jnp.concatenate([keys, values], axis=1)
    everything = lax.all_gather(paired, "ctx", axis=0, tiled=True).reshape(total_blocks, BLK, 2 * head_dim)

    global_blocks = my_index * local_count + jnp.arange(local_count, dtype=jnp.int32)
    chosen = block_lists[global_blocks]
    safe = jnp.maximum(chosen, 0)

    far = everything[safe[:, 1:]]
    own_keys = keys.reshape(local_count, BLK, head_dim)
    own_values = values.reshape(local_count, BLK, head_dim)
    key_sel = jnp.concatenate([own_keys[:, None], far[..., :head_dim]], axis=1)

    q_b = queries.reshape(local_count, BLK, heads, head_dim)
    o_b = output.reshape(local_count, BLK, heads, head_dim)
    g_b = d_output.reshape(local_count, BLK, heads, head_dim)

    raw_own = jnp.einsum("bqhd,bkd->bhqk", q_b, own_keys, preferred_element_type=jnp.float32)
    raw_far = jnp.einsum("bqhd,btkd->bhqtk", q_b, far[..., :head_dim], preferred_element_type=jnp.float32)
    raw = jnp.concatenate([raw_own[:, :, :, None], raw_far], axis=3) * scaling
    query_pos = global_blocks[:, None] * BLK + jnp.arange(BLK, dtype=jnp.int32)[None, :]
    key_pos = safe[:, :, None] * BLK + jnp.arange(BLK, dtype=jnp.int32)[None, None, :]
    allowed = (chosen >= 0)[:, None, :, None] & (key_pos[:, None, :, :] <= query_pos[:, :, None, None])
    scores = jnp.where(allowed[:, None], raw, -jnp.inf)
    top = jnp.max(scores, axis=(3, 4), keepdims=True)
    exps = jnp.exp(scores - top)
    prob = exps / jnp.sum(exps, axis=(3, 4), keepdims=True)

    d_prob_own = jnp.einsum("bqhd,bkd->bhqk", g_b, own_values, preferred_element_type=jnp.float32)
    delta = jnp.sum(g_b.astype(jnp.float32) * o_b.astype(jnp.float32), axis=3)
    delta = jnp.transpose(delta, (0, 2, 1))[:, :, :, None, None]
    prob_rounded = prob.astype(jnp.bfloat16)

    targets = safe.reshape(-1)
    one_hot = (targets[None, :] == jnp.arange(total_blocks, dtype=jnp.int32)[:, None]).astype(jnp.float32)

    def gather_terms(part):
        part = part.reshape(local_count * TOPK, BLK * head_dim)
        terms = jnp.einsum(
            "ns,sx->nx", one_hot, part, precision=lax.Precision.HIGHEST, preferred_element_type=jnp.float32
        )
        return terms.reshape(total_blocks * BLK, head_dim)

    def reduce_terms(terms):
        return lax.psum_scatter(terms, "ctx", scatter_dimension=0, tiled=True)

    value_part = jnp.einsum("bhqtk,bqhd->btkd", prob_rounded, g_b, preferred_element_type=jnp.float32)
    value_terms = gather_terms(value_part)
    value_terms, far_late, g_late = lax.optimization_barrier((value_terms, far, g_b))
    value_mine = reduce_terms(value_terms)

    d_prob_far = jnp.einsum(
        "bqhd,btkd->bhqtk", g_late, far_late[..., head_dim:], preferred_element_type=jnp.float32
    )
    d_prob = jnp.concatenate([d_prob_own[:, :, :, None], d_prob_far], axis=3)
    d_scores = (prob * (d_prob - delta)).astype(jnp.bfloat16)
    key_part = jnp.einsum("bhqtk,bqhd->btkd", d_scores, q_b, preferred_element_type=jnp.float32) * scaling
    key_mine = reduce_terms(gather_terms(key_part))

    d_queries = jnp.einsum("bhqtk,btkd->bqhd", d_scores, key_sel, preferred_element_type=jnp.float32) * scaling
    d_queries = d_queries.astype(jnp.bfloat16).reshape(shard_rows, heads, head_dim)
    return (
        d_queries,
        key_mine.astype(jnp.bfloat16),
        value_mine.astype(jnp.bfloat16),
    )


def solution(mesh):
    return jax.shard_map(
        shards,
        mesh=mesh,
        in_specs=(
            P(("dp", "ctx"), None, None),
            P(("dp", "ctx"), None),
            P(("dp", "ctx"), None),
            P(("dp", "ctx"), None, None),
            P(("dp", "ctx"), None, None),
            P("dp", None),
        ),
        out_specs=(P(("dp", "ctx"), None, None), P(("dp", "ctx"), None), P(("dp", "ctx"), None)),
        check_vma=False,
    )
```

```python
import jax
import jax.numpy as jnp
from jax import lax
from jax.sharding import PartitionSpec as P

BLK = 256
TOPK = 3


def shards(queries, keys, values, output, d_output, block_lists):
    shard_rows, heads, head_dim = queries.shape
    local_count = shard_rows // BLK
    my_index = lax.axis_index("ctx")
    scaling = head_dim ** (-0.5)
    total_blocks = block_lists.shape[0]

    paired = jnp.concatenate([keys, values], axis=1)
    everything = lax.all_gather(paired, "ctx", axis=0, tiled=True).reshape(total_blocks, BLK, 2 * head_dim)

    global_blocks = my_index * local_count + jnp.arange(local_count, dtype=jnp.int32)
    chosen = block_lists[global_blocks]
    safe = jnp.maximum(chosen, 0)

    own_keys = keys.reshape(local_count, BLK, head_dim)
    own_values = values.reshape(local_count, BLK, head_dim)

    q_b = queries.reshape(local_count, BLK, heads, head_dim)
    o_b = output.reshape(local_count, BLK, heads, head_dim)
    g_b = d_output.reshape(local_count, BLK, heads, head_dim)

    raw_own = jnp.einsum("bqhd,bkd->bhqk", q_b, own_keys, preferred_element_type=jnp.float32)
    d_prob_own = jnp.einsum("bqhd,bkd->bhqk", g_b, own_values, preferred_element_type=jnp.float32)
    delta = jnp.sum(g_b.astype(jnp.float32) * o_b.astype(jnp.float32), axis=3)
    everything, raw_own, d_prob_own, delta = lax.optimization_barrier((everything, raw_own, d_prob_own, delta))
    far = everything[safe[:, 1:]]
    key_sel = jnp.concatenate([own_keys[:, None], far[..., :head_dim]], axis=1)
    raw_far = jnp.einsum("bqhd,btkd->bhqtk", q_b, far[..., :head_dim], preferred_element_type=jnp.float32)
    raw = jnp.concatenate([raw_own[:, :, :, None], raw_far], axis=3) * scaling
    query_pos = global_blocks[:, None] * BLK + jnp.arange(BLK, dtype=jnp.int32)[None, :]
    key_pos = safe[:, :, None] * BLK + jnp.arange(BLK, dtype=jnp.int32)[None, None, :]
    allowed = (chosen >= 0)[:, None, :, None] & (key_pos[:, None, :, :] <= query_pos[:, :, None, None])
    scores = jnp.where(allowed[:, None], raw, -jnp.inf)
    top = jnp.max(scores, axis=(3, 4), keepdims=True)
    exps = jnp.exp(scores - top)
    prob = exps / jnp.sum(exps, axis=(3, 4), keepdims=True)

    delta = jnp.transpose(delta, (0, 2, 1))[:, :, :, None, None]
    prob_rounded = prob.astype(jnp.bfloat16)

    targets = safe.reshape(-1)

    def gather_terms(part):
        part = part.reshape(local_count * TOPK, BLK, head_dim)
        terms = jnp.zeros((total_blocks, BLK, head_dim), jnp.float32).at[targets].add(part)
        return terms.reshape(total_blocks * BLK, head_dim)

    def reduce_terms(terms):
        return lax.psum_scatter(terms, "ctx", scatter_dimension=0, tiled=True)

    value_part = jnp.einsum("bhqtk,bqhd->btkd", prob_rounded, g_b, preferred_element_type=jnp.float32)
    value_terms = gather_terms(value_part)
    value_terms, far_late, g_late = lax.optimization_barrier((value_terms, far, g_b))
    value_mine = reduce_terms(value_terms)

    d_prob_far = jnp.einsum(
        "bqhd,btkd->bhqtk", g_late, far_late[..., head_dim:], preferred_element_type=jnp.float32
    )
    d_prob = jnp.concatenate([d_prob_own[:, :, :, None], d_prob_far], axis=3)
    d_scores = (prob * (d_prob - delta)).astype(jnp.bfloat16)
    key_part = jnp.einsum("bhqtk,bqhd->btkd", d_scores, q_b, preferred_element_type=jnp.float32) * scaling
    key_mine = reduce_terms(gather_terms(key_part))

    d_queries = jnp.einsum("bhqtk,btkd->bqhd", d_scores, key_sel, preferred_element_type=jnp.float32) * scaling
    d_queries = d_queries.astype(jnp.bfloat16).reshape(shard_rows, heads, head_dim)
    return (
        d_queries,
        key_mine.astype(jnp.bfloat16),
        value_mine.astype(jnp.bfloat16),
    )


def solution(mesh):
    return jax.shard_map(
        shards,
        mesh=mesh,
        in_specs=(
            P(("dp", "ctx"), None, None),
            P(("dp", "ctx"), None),
            P(("dp", "ctx"), None),
            P(("dp", "ctx"), None, None),
            P(("dp", "ctx"), None, None),
            P("dp", None),
        ),
        out_specs=(P(("dp", "ctx"), None, None), P(("dp", "ctx"), None), P(("dp", "ctx"), None)),
        check_vma=False,
    )
```

```python
import jax
import jax.numpy as jnp
from jax import lax
from jax.sharding import PartitionSpec as P

BLK = 256
TOPK = 3


def shards(queries, keys, values, output, d_output, block_lists):
    shard_rows, heads, head_dim = queries.shape
    local_count = shard_rows // BLK
    my_index = lax.axis_index("ctx")
    scaling = head_dim ** (-0.5)
    total_blocks = block_lists.shape[0]

    paired = jnp.concatenate([keys, values], axis=1)
    everything = lax.all_gather(paired, "ctx", axis=0, tiled=True).reshape(total_blocks, BLK, 2 * head_dim)

    global_blocks = my_index * local_count + jnp.arange(local_count, dtype=jnp.int32)
    chosen = block_lists[global_blocks]
    safe = jnp.maximum(chosen, 0)

    own_keys = keys.reshape(local_count, BLK, head_dim)
    own_values = values.reshape(local_count, BLK, head_dim)

    q_b = queries.reshape(local_count, BLK, heads, head_dim)
    o_b = output.reshape(local_count, BLK, heads, head_dim)
    g_b = d_output.reshape(local_count, BLK, heads, head_dim)

    query_pos = global_blocks[:, None] * BLK + jnp.arange(BLK, dtype=jnp.int32)[None, :]
    key_pos = safe[:, :, None] * BLK + jnp.arange(BLK, dtype=jnp.int32)[None, None, :]
    allowed = (chosen >= 0)[:, None, :, None] & (key_pos[:, None, :, :] <= query_pos[:, :, None, None])

    raw_own = jnp.einsum("bqhd,bkd->bhqk", q_b, own_keys, preferred_element_type=jnp.float32) * scaling
    scores_own = jnp.where(allowed[:, None, :, 0], raw_own, -jnp.inf)
    top_own = jnp.max(scores_own, axis=3)
    d_prob_own = jnp.einsum("bqhd,bkd->bhqk", g_b, own_values, preferred_element_type=jnp.float32)
    delta = jnp.sum(g_b.astype(jnp.float32) * o_b.astype(jnp.float32), axis=3)
    everything, scores_own, top_own, d_prob_own, delta = lax.optimization_barrier(
        (everything, scores_own, top_own, d_prob_own, delta)
    )
    far = everything[safe[:, 1:]]
    key_sel = jnp.concatenate([own_keys[:, None], far[..., :head_dim]], axis=1)
    raw_far = jnp.einsum("bqhd,btkd->bhqtk", q_b, far[..., :head_dim], preferred_element_type=jnp.float32) * scaling
    scores_far = jnp.where(allowed[:, None, :, 1:], raw_far, -jnp.inf)
    top = jnp.maximum(top_own, jnp.max(scores_far, axis=(3, 4)))[:, :, :, None, None]
    scores = jnp.concatenate([scores_own[:, :, :, None], scores_far], axis=3)
    exps = jnp.exp(scores - top)
    prob = exps / jnp.sum(exps, axis=(3, 4), keepdims=True)

    delta = jnp.transpose(delta, (0, 2, 1))[:, :, :, None, None]
    prob_rounded = prob.astype(jnp.bfloat16)

    targets = safe.reshape(-1)

    def gather_terms(part):
        part = part.reshape(local_count * TOPK, BLK, head_dim)
        terms = jnp.zeros((total_blocks, BLK, head_dim), jnp.float32).at[targets].add(part)
        return terms.reshape(total_blocks * BLK, head_dim)

    def reduce_terms(terms):
        return lax.psum_scatter(terms, "ctx", scatter_dimension=0, tiled=True)

    value_part = jnp.einsum("bhqtk,bqhd->btkd", prob_rounded, g_b, preferred_element_type=jnp.float32)
    value_terms = gather_terms(value_part)
    value_terms, far_late, g_late = lax.optimization_barrier((value_terms, far, g_b))
    value_mine = reduce_terms(value_terms)

    d_prob_far = jnp.einsum(
        "bqhd,btkd->bhqtk", g_late, far_late[..., head_dim:], preferred_element_type=jnp.float32
    )
    d_prob = jnp.concatenate([d_prob_own[:, :, :, None], d_prob_far], axis=3)
    d_scores = (prob * (d_prob - delta)).astype(jnp.bfloat16)
    key_part = jnp.einsum("bhqtk,bqhd->btkd", d_scores, q_b, preferred_element_type=jnp.float32) * scaling
    key_mine = reduce_terms(gather_terms(key_part))

    d_queries = jnp.einsum("bhqtk,btkd->bqhd", d_scores, key_sel, preferred_element_type=jnp.float32) * scaling
    d_queries = d_queries.astype(jnp.bfloat16).reshape(shard_rows, heads, head_dim)
    return (
        d_queries,
        key_mine.astype(jnp.bfloat16),
        value_mine.astype(jnp.bfloat16),
    )


def solution(mesh):
    return jax.shard_map(
        shards,
        mesh=mesh,
        in_specs=(
            P(("dp", "ctx"), None, None),
            P(("dp", "ctx"), None),
            P(("dp", "ctx"), None),
            P(("dp", "ctx"), None, None),
            P(("dp", "ctx"), None, None),
            P("dp", None),
        ),
        out_specs=(P(("dp", "ctx"), None, None), P(("dp", "ctx"), None), P(("dp", "ctx"), None)),
        check_vma=False,
    )
```

```python
import jax
import jax.numpy as jnp
from jax import lax
from jax.sharding import PartitionSpec as P

BLK = 256
TOPK = 3


def shards(queries, keys, values, output, d_output, block_lists):
    shard_rows, heads, head_dim = queries.shape
    local_count = shard_rows // BLK
    my_index = lax.axis_index("ctx")
    scaling = head_dim ** (-0.5)
    total_blocks = block_lists.shape[0]

    paired = jnp.concatenate([keys, values], axis=1)
    everything = lax.all_gather(paired, "ctx", axis=0, tiled=True).reshape(total_blocks, BLK, 2 * head_dim)

    global_blocks = my_index * local_count + jnp.arange(local_count, dtype=jnp.int32)
    chosen = block_lists[global_blocks]
    safe = jnp.maximum(chosen, 0)

    own_keys = keys.reshape(local_count, BLK, head_dim)
    own_values = values.reshape(local_count, BLK, head_dim)

    q_b = queries.reshape(local_count, BLK, heads, head_dim)
    o_b = output.reshape(local_count, BLK, heads, head_dim)
    g_b = d_output.reshape(local_count, BLK, heads, head_dim)

    query_pos = global_blocks[:, None] * BLK + jnp.arange(BLK, dtype=jnp.int32)[None, :]
    key_pos = safe[:, :, None] * BLK + jnp.arange(BLK, dtype=jnp.int32)[None, None, :]
    allowed = (chosen >= 0)[:, None, :, None] & (key_pos[:, None, :, :] <= query_pos[:, :, None, None])

    raw_own = jnp.einsum("bqhd,bkd->bhqk", q_b, own_keys, preferred_element_type=jnp.float32) * scaling
    scores_own = jnp.where(allowed[:, None, :, 0], raw_own, -jnp.inf)
    top_own = jnp.max(scores_own, axis=3)
    d_prob_own = jnp.einsum("bqhd,bkd->bhqk", g_b, own_values, preferred_element_type=jnp.float32)
    delta = jnp.sum(g_b.astype(jnp.float32) * o_b.astype(jnp.float32), axis=3)
    value_zeros = jnp.zeros((total_blocks, BLK, head_dim), jnp.float32)
    scores_own, top_own, value_zeros = lax.optimization_barrier((scores_own, top_own, value_zeros))
    everything, scores_own, top_own, d_prob_own, delta = lax.optimization_barrier(
        (everything, scores_own, top_own, d_prob_own, delta)
    )
    far = everything[safe[:, 1:]]
    key_sel = jnp.concatenate([own_keys[:, None], far[..., :head_dim]], axis=1)
    raw_far = jnp.einsum("bqhd,btkd->bhqtk", q_b, far[..., :head_dim], preferred_element_type=jnp.float32) * scaling
    scores_far = jnp.where(allowed[:, None, :, 1:], raw_far, -jnp.inf)
    top = jnp.maximum(top_own, jnp.max(scores_far, axis=(3, 4)))[:, :, :, None, None]
    scores = jnp.concatenate([scores_own[:, :, :, None], scores_far], axis=3)
    exps = jnp.exp(scores - top)
    prob = exps / jnp.sum(exps, axis=(3, 4), keepdims=True)

    delta = jnp.transpose(delta, (0, 2, 1))[:, :, :, None, None]
    prob_rounded = prob.astype(jnp.bfloat16)

    targets = safe.reshape(-1)

    def gather_terms(part, zeros):
        part = part.reshape(local_count * TOPK, BLK, head_dim)
        terms = zeros.at[targets].add(part)
        return terms.reshape(total_blocks * BLK, head_dim)

    def reduce_terms(terms):
        return lax.psum_scatter(terms, "ctx", scatter_dimension=0, tiled=True)

    value_part = jnp.einsum("bhqtk,bqhd->btkd", prob_rounded, g_b, preferred_element_type=jnp.float32)
    value_terms = gather_terms(value_part, value_zeros)
    value_terms, far_late, g_late = lax.optimization_barrier((value_terms, far, g_b))
    value_mine = reduce_terms(value_terms)

    d_prob_far = jnp.einsum(
        "bqhd,btkd->bhqtk", g_late, far_late[..., head_dim:], preferred_element_type=jnp.float32
    )
    d_prob = jnp.concatenate([d_prob_own[:, :, :, None], d_prob_far], axis=3)
    d_scores = (prob * (d_prob - delta)).astype(jnp.bfloat16)
    key_part = jnp.einsum("bhqtk,bqhd->btkd", d_scores, q_b, preferred_element_type=jnp.float32) * scaling
    key_mine = reduce_terms(gather_terms(key_part, jnp.zeros((total_blocks, BLK, head_dim), jnp.float32)))

    d_queries = jnp.einsum("bhqtk,btkd->bqhd", d_scores, key_sel, preferred_element_type=jnp.float32) * scaling
    d_queries = d_queries.astype(jnp.bfloat16).reshape(shard_rows, heads, head_dim)
    return (
        d_queries,
        key_mine.astype(jnp.bfloat16),
        value_mine.astype(jnp.bfloat16),
    )


def solution(mesh):
    return jax.shard_map(
        shards,
        mesh=mesh,
        in_specs=(
            P(("dp", "ctx"), None, None),
            P(("dp", "ctx"), None),
            P(("dp", "ctx"), None),
            P(("dp", "ctx"), None, None),
            P(("dp", "ctx"), None, None),
            P("dp", None),
        ),
        out_specs=(P(("dp", "ctx"), None, None), P(("dp", "ctx"), None), P(("dp", "ctx"), None)),
        check_vma=False,
    )
```

```python
import jax
import jax.numpy as jnp
from jax import lax
from jax.sharding import PartitionSpec as P

BLK = 256
TOPK = 3


def shards(queries, keys, values, output, d_output, block_lists):
    shard_rows, heads, head_dim = queries.shape
    local_count = shard_rows // BLK
    my_index = lax.axis_index("ctx")
    scaling = head_dim ** (-0.5)
    total_blocks = block_lists.shape[0]

    paired = jnp.concatenate([keys, values], axis=1)
    everything = lax.all_gather(paired, "ctx", axis=0, tiled=True).reshape(total_blocks, BLK, 2 * head_dim)

    global_blocks = my_index * local_count + jnp.arange(local_count, dtype=jnp.int32)
    chosen = block_lists[global_blocks]
    safe = jnp.maximum(chosen, 0)

    own_keys = keys.reshape(local_count, BLK, head_dim)
    own_values = values.reshape(local_count, BLK, head_dim)

    q_b = queries.reshape(local_count, BLK, heads, head_dim)
    o_b = output.reshape(local_count, BLK, heads, head_dim)
    g_b = d_output.reshape(local_count, BLK, heads, head_dim)

    query_pos = global_blocks[:, None] * BLK + jnp.arange(BLK, dtype=jnp.int32)[None, :]
    key_pos = safe[:, :, None] * BLK + jnp.arange(BLK, dtype=jnp.int32)[None, None, :]
    allowed = (chosen >= 0)[:, None, :, None] & (key_pos[:, None, :, :] <= query_pos[:, :, None, None])

    raw_own = jnp.einsum("bqhd,bkd->bhqk", q_b, own_keys, preferred_element_type=jnp.float32) * scaling
    scores_own = jnp.where(allowed[:, None, :, 0], raw_own, -jnp.inf)
    top_own = jnp.max(scores_own, axis=3)
    d_prob_own = jnp.einsum("bqhd,bkd->bhqk", g_b, own_values, preferred_element_type=jnp.float32)
    delta = jnp.sum(g_b.astype(jnp.float32) * o_b.astype(jnp.float32), axis=3)
    value_zeros = jnp.zeros((total_blocks, BLK, head_dim), jnp.float32)
    scores_own, top_own, value_zeros = lax.optimization_barrier((scores_own, top_own, value_zeros))
    everything, scores_own, top_own, d_prob_own, delta = lax.optimization_barrier(
        (everything, scores_own, top_own, d_prob_own, delta)
    )
    far = jnp.stack(
        [
            jnp.stack([lax.dynamic_index_in_dim(everything, safe[lb, t], 0, keepdims=False) for t in range(1, TOPK)])
            for lb in range(local_count)
        ]
    )
    key_sel = jnp.concatenate([own_keys[:, None], far[..., :head_dim]], axis=1)
    raw_far = jnp.einsum("bqhd,btkd->bhqtk", q_b, far[..., :head_dim], preferred_element_type=jnp.float32) * scaling
    scores_far = jnp.where(allowed[:, None, :, 1:], raw_far, -jnp.inf)
    top = jnp.maximum(top_own, jnp.max(scores_far, axis=(3, 4)))[:, :, :, None, None]
    scores = jnp.concatenate([scores_own[:, :, :, None], scores_far], axis=3)
    exps = jnp.exp(scores - top)
    prob = exps / jnp.sum(exps, axis=(3, 4), keepdims=True)

    delta = jnp.transpose(delta, (0, 2, 1))[:, :, :, None, None]
    prob_rounded = prob.astype(jnp.bfloat16)

    targets = safe.reshape(-1)

    def gather_terms(part, zeros):
        part = part.reshape(local_count * TOPK, BLK, head_dim)
        terms = zeros.at[targets].add(part)
        return terms.reshape(total_blocks * BLK, head_dim)

    def reduce_terms(terms):
        return lax.psum_scatter(terms, "ctx", scatter_dimension=0, tiled=True)

    value_part = jnp.einsum("bhqtk,bqhd->btkd", prob_rounded, g_b, preferred_element_type=jnp.float32)
    value_terms = gather_terms(value_part, value_zeros)
    value_terms, far_late, g_late = lax.optimization_barrier((value_terms, far, g_b))
    value_mine = reduce_terms(value_terms)

    d_prob_far = jnp.einsum(
        "bqhd,btkd->bhqtk", g_late, far_late[..., head_dim:], preferred_element_type=jnp.float32
    )
    d_prob = jnp.concatenate([d_prob_own[:, :, :, None], d_prob_far], axis=3)
    d_scores = (prob * (d_prob - delta)).astype(jnp.bfloat16)
    key_part = jnp.einsum("bhqtk,bqhd->btkd", d_scores, q_b, preferred_element_type=jnp.float32) * scaling
    key_mine = reduce_terms(gather_terms(key_part, jnp.zeros((total_blocks, BLK, head_dim), jnp.float32)))

    d_queries = jnp.einsum("bhqtk,btkd->bqhd", d_scores, key_sel, preferred_element_type=jnp.float32) * scaling
    d_queries = d_queries.astype(jnp.bfloat16).reshape(shard_rows, heads, head_dim)
    return (
        d_queries,
        key_mine.astype(jnp.bfloat16),
        value_mine.astype(jnp.bfloat16),
    )


def solution(mesh):
    return jax.shard_map(
        shards,
        mesh=mesh,
        in_specs=(
            P(("dp", "ctx"), None, None),
            P(("dp", "ctx"), None),
            P(("dp", "ctx"), None),
            P(("dp", "ctx"), None, None),
            P(("dp", "ctx"), None, None),
            P("dp", None),
        ),
        out_specs=(P(("dp", "ctx"), None, None), P(("dp", "ctx"), None), P(("dp", "ctx"), None)),
        check_vma=False,
    )
```
